512 devices in a mesh: dp: 16 (over x, y_hi, core), tensor: 32 (over y_lo, z).
Axes of the slice: x: 4, y: 8 (y_hi: 2, y_lo: 4; y = y_hi * 4 + y_lo), z: 8, core: 2. Of those that a mesh axis runs over, the one named last changes fastest.
Arguments:
- tokens: bfloat16 [8192, 8192], P('dp', 'tensor'), may hold values from -6 to 6
- first_right: bfloat16 [32, 256, 1024], P('tensor'), may hold values from -0.375 to 0.375
- first_left: bfloat16 [128, 256, 256], P('tensor'), may hold values from -0.375 to 0.375
- second_right: bfloat16 [128, 256, 256], P('tensor'), may hold values from -0.375 to 0.375
- second_left: bfloat16 [32, 1024, 256], P('tensor'), may hold values from -0.1875 to 0.1875
- cotangent: bfloat16 [8192, 8192], P('dp', 'tensor'), may hold values from -6 to 6
Outputs:
- layer_out: bfloat16 [8192, 8192], P('dp', 'tensor')
- grad_tokens: bfloat16 [8192, 8192], P('dp', 'tensor')
- grad_first_right: float32 [32, 256, 1024], P('tensor', 'dp')
- grad_first_left: float32 [128, 256, 256], P('tensor', 'dp')
- grad_second_right: float32 [128, 256, 256], P('tensor', 'dp')
- grad_second_left: float32 [32, 1024, 256], P('tensor', 'dp')
The draws below stay inside these ranges and needn't reach their ends.
All inputs are finite; a program needn't handle non-finite values.
Results may differ from the reference program's by a relative error of at most 0.018.
Values may be sent and summed in bfloat16 or wider, within the bound.
No kernel may reach another device: no remote copies, remote signals or barrier semaphores. Data moves between devices by JAX's collectives and lax.ppermute only.
A program may use at most 64 MiB of HBM per device.

```python
import jax
import jax.numpy as jnp
from jax import lax

D = 8192
BLK = 256
TOK_DEV = 512
NB_IN = 32
NB_HID = 128
WIDE = 1024
SUB = 8
TOKENS = 8192
N_DP = 16


def block_levels(rng, shape, pieces, smallest, top_value):
    def one(position, blocks):
        draws = jax.random.uniform(jax.random.fold_in(jax.random.fold_in(rng, 6), position), (blocks,), jnp.float32, smallest / len(pieces), top_value / len(pieces))
        return jnp.repeat(jnp.exp(draws), shape[position] // blocks).reshape((-1,) + (1,) * (len(shape) - position - 1))

    level = one(*pieces[0])
    for cut in pieces[1:]:
        level = level * one(*cut)
    return level


def normal_values(rng, extent, scale, reach, split=(), dtype=jnp.bfloat16):
    drawn = scale * jax.random.normal(rng, extent, jnp.float32)
    if split:
        drawn = drawn * block_levels(rng, extent, split, -0.22, 0.18)
    return jnp.clip(drawn, -reach, reach).astype(dtype)


def setup_inputs(seed: int = 0) -> dict:
    seeds = jax.random.split(jax.random.key(seed), 7)
    return {
        "tokens": normal_values(seeds[0], (TOKENS, D), 1.0, 6.0, ((0, 16), (1, 32))),
        "first_right": normal_values(seeds[1], (NB_IN, BLK, WIDE), BLK ** -0.5, 0.375, ((0, 32),)),
        "first_left": normal_values(seeds[2], (NB_HID, BLK, BLK), BLK ** -0.5, 0.375, ((0, 32),)),
        "second_right": normal_values(seeds[3], (NB_HID, BLK, BLK), BLK ** -0.5, 0.375, ((0, 32),)),
        "second_left": normal_values(seeds[4], (NB_IN, WIDE, BLK), WIDE ** -0.5, 0.1875, ((0, 32),)),
        "cotangent": normal_values(seeds[5], (TOKENS, D), 1.0, 6.0, ((0, 16), (1, 32))),
    }


half_root = 0.7071067811865476
inv_root_two_pi = 0.3989422804014327


def gelu_value(value):
    return 0.5 * value * (1.0 + jax.scipy.special.erf(value * half_root))


def gelu_slope(value):
    return 0.5 * (1.0 + jax.scipy.special.erf(value * half_root)) + value * jnp.exp(-0.5 * value * value) * inv_root_two_pi


def reference(tokens, first_right, first_left, second_right, second_left, cotangent):
    fp = jnp.float32
    bf = jnp.bfloat16
    grad_scale = float(TOKENS) ** -0.5
    right_one = first_right.astype(fp).reshape(NB_IN, BLK, NB_HID, SUB)
    left_one = first_left.astype(fp)
    right_two = second_right.astype(fp).reshape(NB_HID, BLK, NB_IN, SUB)
    left_two = second_left.astype(fp)

    def one_block(carry, inputs):
        tok_block, cot_block = inputs
        tok_rows = tok_block.shape[0]
        tok_parts = tok_block.astype(fp).reshape(tok_rows, NB_IN, BLK)
        up_inner = jnp.einsum('tkb,kbjg->jtkg', tok_parts, right_one).astype(bf)
        mixed_up = up_inner.reshape(NB_HID, tok_rows, BLK).astype(fp)
        pre_act = jnp.einsum('jtb,jbc->jtc', mixed_up, left_one)
        hidden = gelu_value(pre_act).astype(bf).astype(fp)
        down_inner = jnp.einsum('jtb,jbkg->ktjg', hidden, right_two).astype(bf)
        mixed_down = down_inner.reshape(NB_IN, tok_rows, WIDE).astype(fp)
        out_block = jnp.einsum('ktw,kwc->tkc', mixed_down, left_two).astype(bf).reshape(tok_rows, D)
        cot_parts = cot_block.astype(fp).reshape(tok_rows, NB_IN, BLK)
        d_mixed_down = jnp.einsum('tkc,kwc->ktw', cot_parts, left_two).astype(bf).astype(fp)
        d_down_inner = d_mixed_down.reshape(NB_IN, tok_rows, NB_HID, SUB)
        d_hidden = jnp.einsum('ktjg,jbkg->jtb', d_down_inner, right_two)
        d_pre = (d_hidden * gelu_slope(pre_act)).astype(bf).astype(fp)
        d_mixed_up = jnp.einsum('jtc,jbc->jtb', d_pre, left_one).astype(bf).astype(fp)
        d_up_inner = d_mixed_up.reshape(NB_HID, tok_rows, NB_IN, SUB)
        grad_block = jnp.einsum('jtkg,kbjg->tkb', d_up_inner, right_one).astype(bf).reshape(tok_rows, D)
        grad_left_two = jnp.einsum('ktw,tkc->kwc', mixed_down, cot_parts) * grad_scale
        grad_right_two = jnp.einsum('jtb,ktjg->jbkg', hidden, d_down_inner).reshape(NB_HID, BLK, BLK) * grad_scale
        grad_left_one = jnp.einsum('jtb,jtc->jbc', mixed_up, d_pre) * grad_scale
        grad_right_one = jnp.einsum('tkb,jtkg->kbjg', tok_parts, d_up_inner).reshape(NB_IN, BLK, WIDE) * grad_scale
        totals = (carry[0] + grad_right_one, carry[1] + grad_left_one, carry[2] + grad_right_two, carry[3] + grad_left_two)
        return totals, (out_block, grad_block)

    start = (jnp.zeros((NB_IN, BLK, WIDE), fp), jnp.zeros((NB_HID, BLK, BLK), fp),
             jnp.zeros((NB_HID, BLK, BLK), fp), jnp.zeros((NB_IN, WIDE, BLK), fp))
    tok_split = tokens.reshape(N_DP, TOK_DEV, D)
    cot_split = cotangent.reshape(N_DP, TOK_DEV, D)
    totals, stacked = lax.scan(one_block, start, (tok_split, cot_split))
    layer_out = stacked[0].reshape(TOKENS, D)
    grad_tokens = stacked[1].reshape(TOKENS, D)
    return layer_out, grad_tokens, totals[0], totals[1], totals[2], totals[3]
```

```python
import jax
import jax.numpy as jnp
from jax import lax
from jax.sharding import PartitionSpec as P

half_root = 0.7071067811865476
inv_root_two_pi = 0.3989422804014327


def gelu_value(value):
    return 0.5 * value * (1.0 + jax.scipy.special.erf(value * half_root))


def gelu_slope(value):
    return (
        0.5 * (1.0 + jax.scipy.special.erf(value * half_root))
        + value * jnp.exp(-0.5 * value * value) * inv_root_two_pi
    )


def dp_bit_order(replicas):
    bits = replicas.bit_length() - 1
    assert 1 << bits == replicas
    preferred = [0, 2, 3, 1]
    if bits == 4:
        return preferred
    return list(range(bits))


def dp_reduce_scatter(buf, replicas):
    idx = lax.axis_index("dp")
    order = dp_bit_order(replicas)
    bits = len(order)
    width = buf.shape[1]
    buf = buf.reshape((2,) * bits + (width,))
    live = list(range(bits - 1, -1, -1))
    for bit in order:
        axis = live.index(bit)
        me = (idx >> bit) & 1
        keep = lax.dynamic_index_in_dim(buf, me, axis, keepdims=False)
        send = lax.dynamic_index_in_dim(buf, 1 - me, axis, keepdims=False)
        perm = [(i, i ^ (1 << bit)) for i in range(replicas)]
        got = lax.ppermute(send.astype(jnp.bfloat16), "dp", perm)
        buf = keep + got.astype(jnp.float32)
        live.pop(axis)
    return buf.reshape(width)


def shards(tokens, first_right, first_left, second_right, second_left, cotangent):
    fp = jnp.float32
    bf = jnp.bfloat16
    tok_rows = tokens.shape[0]
    in_blocks = first_right.shape[0]
    block_width = first_right.shape[1]
    wide_width = first_right.shape[2]
    hid_blocks = first_left.shape[0]
    groups = lax.axis_size("tensor")
    replicas = lax.axis_size("dp")
    all_in = in_blocks * groups
    all_hid = hid_blocks * groups
    sub_width = wide_width // all_hid
    grad_scale = float(tok_rows * replicas) ** (-0.5)
    right_one = first_right.reshape(in_blocks, block_width, all_hid, sub_width)
    right_two = second_right.reshape(hid_blocks, block_width, all_in, sub_width)
    tok_parts = tokens.reshape(tok_rows, in_blocks, block_width)
    cot_parts = cotangent.reshape(tok_rows, in_blocks, block_width)
    up_inner = jnp.einsum("tkb,kbjg->jkgt", tok_parts, right_one, preferred_element_type=fp).astype(
        bf
    )
    arrived = lax.all_to_all(up_inner, "tensor", split_axis=0, concat_axis=1, tiled=True)
    mixed_piece = arrived.reshape(hid_blocks, block_width, arrived.shape[3])
    pre_piece = jnp.einsum("jbt,jbc->jct", mixed_piece, first_left, preferred_element_type=fp)
    hidden = gelu_value(pre_piece).astype(bf)
    down_inner = jnp.einsum("jbt,jbkg->kjgt", hidden, right_two, preferred_element_type=fp).astype(
        bf
    )
    mixed_down = lax.all_to_all(down_inner, "tensor", split_axis=0, concat_axis=1, tiled=True)
    mixed_down = mixed_down.reshape(in_blocks, wide_width, tok_rows)
    layer_out = jnp.einsum(
        "kwt,kwc->tkc", mixed_down, second_left, preferred_element_type=fp
    ).astype(bf)
    layer_out = layer_out.reshape(tok_rows, in_blocks * block_width)
    reduced = {}
    d_mixed_down = jnp.einsum(
        "tkc,kwc->kwt", cot_parts, second_left, preferred_element_type=fp
    ).astype(bf)
    d_mixed_down = d_mixed_down.reshape(in_blocks, all_hid, sub_width, tok_rows)
    d_down_inner = lax.all_to_all(d_mixed_down, "tensor", split_axis=1, concat_axis=0, tiled=True)
    d_hidden = jnp.einsum("kjgt,jbkg->jbt", d_down_inner, right_two, preferred_element_type=fp)
    d_pre = (d_hidden * gelu_slope(pre_piece)).astype(bf)
    d_mixed_up = jnp.einsum("jct,jbc->jbt", d_pre, first_left, preferred_element_type=fp).astype(bf)
    d_mixed_up = d_mixed_up.reshape(hid_blocks, all_in, sub_width, tok_rows)
    d_up_inner = lax.all_to_all(d_mixed_up, "tensor", split_axis=1, concat_axis=0, tiled=True)
    grad_tokens = jnp.einsum(
        "jkgt,kbjg->tkb", d_up_inner, right_one, preferred_element_type=fp
    ).astype(bf)
    grad_tokens = grad_tokens.reshape(tok_rows, in_blocks * block_width)
    grads = (
        jnp.einsum("tkb,jkgt->bkjg", tok_parts, d_up_inner, preferred_element_type=fp),
        jnp.einsum("jbt,jct->bjc", mixed_piece, d_pre, preferred_element_type=fp),
        jnp.einsum("jbt,kjgt->bjkg", hidden, d_down_inner, preferred_element_type=fp),
        jnp.einsum("kwt,tkc->wkc", mixed_down, cot_parts, preferred_element_type=fp),
    )
    pieces = [g.reshape(replicas, -1) for g in grads]
    widths = [p.shape[1] for p in pieces]
    total = dp_reduce_scatter(jnp.concatenate(pieces, axis=1), replicas) * grad_scale
    outs = []
    offset = 0
    for g, w in zip(grads, widths):
        part = total[offset : offset + w]
        offset += w
        lead = g.shape[0] // replicas
        outs.append(jnp.transpose(part.reshape(lead, g.shape[1], -1), (1, 0, 2)))
    grad_right_one, grad_left_one, grad_right_two, grad_left_two = outs
    return (layer_out, grad_tokens, grad_right_one, grad_left_one, grad_right_two, grad_left_two)


def solution(mesh):
    in_specs = (
        P("dp", "tensor"),
        P("tensor", None, None),
        P("tensor", None, None),
        P("tensor", None, None),
        P("tensor", None, None),
        P("dp", "tensor"),
    )
    out_specs = (
        P("dp", "tensor"),
        P("dp", "tensor"),
        P("tensor", "dp", None),
        P("tensor", "dp", None),
        P("tensor", "dp", None),
        P("tensor", "dp", None),
    )
    return jax.shard_map(shards, mesh=mesh, in_specs=in_specs, out_specs=out_specs, check_vma=False)
```

```python
import jax
import jax.numpy as jnp
from jax import lax
from jax.sharding import PartitionSpec as P

half_root = 0.7071067811865476
inv_root_two_pi = 0.3989422804014327


def gelu_value(value):
    return 0.5 * value * (1.0 + jax.scipy.special.erf(value * half_root))


def gelu_slope(value):
    return (
        0.5 * (1.0 + jax.scipy.special.erf(value * half_root))
        + value * jnp.exp(-0.5 * value * value) * inv_root_two_pi
    )


def dp_bit_order(replicas):
    bits = replicas.bit_length() - 1
    assert 1 << bits == replicas
    preferred = [0, 2, 3, 1]
    if bits == 4:
        return preferred
    return list(range(bits))


def dp_reduce_scatter(arrays, replicas):
    idx = lax.axis_index("dp")
    order = dp_bit_order(replicas)
    bits = len(order)
    views = [a.reshape(a.shape[:1] + (2,) * bits + a.shape[2:]) for a in arrays]
    live = list(range(bits - 1, -1, -1))
    for bit in order:
        axis = 1 + live.index(bit)
        me = (idx >> bit) & 1
        keeps = [lax.dynamic_index_in_dim(v, me, axis, keepdims=False) for v in views]
        sends = [lax.dynamic_index_in_dim(v, 1 - me, axis, keepdims=False) for v in views]
        packed = jnp.concatenate([s.astype(jnp.bfloat16).reshape(-1) for s in sends])
        perm = [(i, i ^ (1 << bit)) for i in range(replicas)]
        got = lax.ppermute(packed, "dp", perm)
        views = []
        offset = 0
        for k in keeps:
            n = k.size
            views.append(k + got[offset : offset + n].reshape(k.shape).astype(jnp.float32))
            offset += n
        live.pop(axis - 1)
    return views


def shards(tokens, first_right, first_left, second_right, second_left, cotangent):
    fp = jnp.float32
    bf = jnp.bfloat16
    tok_rows = tokens.shape[0]
    in_blocks = first_right.shape[0]
    block_width = first_right.shape[1]
    wide_width = first_right.shape[2]
    hid_blocks = first_left.shape[0]
    groups = lax.axis_size("tensor")
    replicas = lax.axis_size("dp")
    all_in = in_blocks * groups
    all_hid = hid_blocks * groups
    sub_width = wide_width // all_hid
    grad_scale = float(tok_rows * replicas) ** (-0.5)
    right_one = first_right.reshape(in_blocks, block_width, all_hid, sub_width)
    right_two = second_right.reshape(hid_blocks, block_width, all_in, sub_width)
    tok_parts = tokens.reshape(tok_rows, in_blocks, block_width)
    cot_parts = cotangent.reshape(tok_rows, in_blocks, block_width)
    up_inner = jnp.einsum("tkb,kbjg->jkgt", tok_parts, right_one, preferred_element_type=fp).astype(
        bf
    )
    arrived = lax.all_to_all(up_inner, "tensor", split_axis=0, concat_axis=1, tiled=True)
    mixed_piece = arrived.reshape(hid_blocks, block_width, arrived.shape[3])
    pre_piece = jnp.einsum("jbt,jbc->jct", mixed_piece, first_left, preferred_element_type=fp)
    hidden = gelu_value(pre_piece).astype(bf)
    down_inner = jnp.einsum("jbt,jbkg->kjgt", hidden, right_two, preferred_element_type=fp).astype(
        bf
    )
    mixed_down = lax.all_to_all(down_inner, "tensor", split_axis=0, concat_axis=1, tiled=True)
    mixed_down = mixed_down.reshape(in_blocks, wide_width, tok_rows)
    layer_out = jnp.einsum(
        "kwt,kwc->tkc", mixed_down, second_left, preferred_element_type=fp
    ).astype(bf)
    layer_out = layer_out.reshape(tok_rows, in_blocks * block_width)
    reduced = {}
    d_mixed_down = jnp.einsum(
        "tkc,kwc->kwt", cot_parts, second_left, preferred_element_type=fp
    ).astype(bf)
    d_mixed_down = d_mixed_down.reshape(in_blocks, all_hid, sub_width, tok_rows)
    d_down_inner = lax.all_to_all(d_mixed_down, "tensor", split_axis=1, concat_axis=0, tiled=True)
    d_hidden = jnp.einsum("kjgt,jbkg->jbt", d_down_inner, right_two, preferred_element_type=fp)
    d_pre = (d_hidden * gelu_slope(pre_piece)).astype(bf)
    d_mixed_up = jnp.einsum("jct,jbc->jbt", d_pre, first_left, preferred_element_type=fp).astype(bf)
    d_mixed_up = d_mixed_up.reshape(hid_blocks, all_in, sub_width, tok_rows)
    d_up_inner = lax.all_to_all(d_mixed_up, "tensor", split_axis=1, concat_axis=0, tiled=True)
    grad_tokens = jnp.einsum(
        "jkgt,kbjg->tkb", d_up_inner, right_one, preferred_element_type=fp
    ).astype(bf)
    grad_tokens = grad_tokens.reshape(tok_rows, in_blocks * block_width)
    d_up_flat = d_up_inner.reshape(all_hid * in_blocks * sub_width, tok_rows)
    grads = (
        jnp.einsum("tb,nt->bn", tok_parts[:, 0, :], d_up_flat, preferred_element_type=fp).reshape(
            in_blocks, block_width, wide_width
        ),
        jnp.einsum("jbt,jct->jbc", mixed_piece, d_pre, preferred_element_type=fp),
        jnp.einsum("jbt,kjgt->jbkg", hidden, d_down_inner, preferred_element_type=fp).reshape(
            hid_blocks, block_width, block_width
        ),
        jnp.einsum("kwt,tkc->kwc", mixed_down, cot_parts, preferred_element_type=fp),
    )
    views = [g.reshape(g.shape[0], replicas, g.shape[1] // replicas, g.shape[2]) for g in grads]
    reduced = dp_reduce_scatter(views, replicas)
    grad_right_one, grad_left_one, grad_right_two, grad_left_two = [r * grad_scale for r in reduced]
    return (layer_out, grad_tokens, grad_right_one, grad_left_one, grad_right_two, grad_left_two)


def solution(mesh):
    in_specs = (
        P("dp", "tensor"),
        P("tensor", None, None),
        P("tensor", None, None),
        P("tensor", None, None),
        P("tensor", None, None),
        P("dp", "tensor"),
    )
    out_specs = (
        P("dp", "tensor"),
        P("dp", "tensor"),
        P("tensor", "dp", None),
        P("tensor", "dp", None),
        P("tensor", "dp", None),
        P("tensor", "dp", None),
    )
    return jax.shard_map(shards, mesh=mesh, in_specs=in_specs, out_specs=out_specs, check_vma=False)
```

```python
import jax
import jax.numpy as jnp
from jax import lax
from jax.sharding import PartitionSpec as P

half_root = 0.7071067811865476
inv_root_two_pi = 0.3989422804014327


def gelu_value(value):
    return 0.5 * value * (1.0 + jax.scipy.special.erf(value * half_root))


def gelu_slope(value):
    return (
        0.5 * (1.0 + jax.scipy.special.erf(value * half_root))
        + value * jnp.exp(-0.5 * value * value) * inv_root_two_pi
    )


def dp_bit_order(replicas):
    bits = replicas.bit_length() - 1
    assert 1 << bits == replicas
    preferred = [0, 2, 3, 1]
    if bits == 4:
        return preferred
    return list(range(bits))


def chunk_order(x, axis, replicas):
    order = dp_bit_order(replicas)
    bits = len(order)
    shape = x.shape
    view = x.reshape(shape[:axis] + (2,) * bits + (shape[axis] // replicas,) + shape[axis + 1 :])
    moved = [axis + bits - 1 - b for b in order]
    perm = list(range(axis)) + moved + list(range(axis + bits, view.ndim))
    return jnp.transpose(view, perm).reshape(shape)


def dp_reduce_scatter(wide, narrow, replicas):
    idx = lax.axis_index("dp")
    order = dp_bit_order(replicas)
    arrays = [wide] + list(narrow)
    size = replicas
    for bit in order:
        half = size // 2
        me = (idx >> bit) & 1
        keeps = [lax.dynamic_slice_in_dim(a, me * half, half, axis=1) for a in arrays]
        sends = [lax.dynamic_slice_in_dim(a, (1 - me) * half, half, axis=1) for a in arrays]
        sends = [s.astype(jnp.bfloat16) for s in sends]
        first = sends[0].reshape(-1, sends[0].shape[-1])
        rest = jnp.concatenate([s.reshape(-1, s.shape[-1]) for s in sends[1:]], axis=0)
        perm = [(i, i ^ (1 << bit)) for i in range(replicas)]
        got_first, got_rest = lax.ppermute((first, rest), "dp", perm)
        arrays = [keeps[0] + got_first.reshape(keeps[0].shape).astype(jnp.float32)]
        offset = 0
        for k in keeps[1:]:
            rows = k.size // k.shape[-1]
            part = got_rest[offset : offset + rows].reshape(k.shape)
            arrays.append(k + part.astype(jnp.float32))
            offset += rows
        size = half
    return [a.reshape(a.shape[:1] + a.shape[2:]) for a in arrays]


def shards(tokens, first_right, first_left, second_right, second_left, cotangent):
    fp = jnp.float32
    bf = jnp.bfloat16
    tok_rows = tokens.shape[0]
    in_blocks = first_right.shape[0]
    block_width = first_right.shape[1]
    wide_width = first_right.shape[2]
    hid_blocks = first_left.shape[0]
    groups = lax.axis_size("tensor")
    replicas = lax.axis_size("dp")
    all_in = in_blocks * groups
    all_hid = hid_blocks * groups
    sub_width = wide_width // all_hid
    grad_scale = float(tok_rows * replicas) ** (-0.5)
    right_one = first_right.reshape(in_blocks, block_width, all_hid, sub_width)
    right_two = second_right.reshape(hid_blocks, block_width, all_in, sub_width)
    tok_parts = tokens.reshape(tok_rows, in_blocks, block_width)
    cot_parts = cotangent.reshape(tok_rows, in_blocks, block_width)
    up_inner = jnp.einsum("tkb,kbjg->jkgt", tok_parts, right_one, preferred_element_type=fp).astype(
        bf
    )
    arrived = lax.all_to_all(up_inner, "tensor", split_axis=0, concat_axis=1, tiled=True)
    mixed_piece = arrived.reshape(hid_blocks, block_width, arrived.shape[3])
    pre_piece = jnp.einsum("jbt,jbc->jct", mixed_piece, first_left, preferred_element_type=fp)
    hidden = gelu_value(pre_piece).astype(bf)
    down_inner = jnp.einsum("jbt,jbkg->kjgt", hidden, right_two, preferred_element_type=fp).astype(
        bf
    )
    mixed_down = lax.all_to_all(down_inner, "tensor", split_axis=0, concat_axis=1, tiled=True)
    mixed_down = mixed_down.reshape(in_blocks, wide_width, tok_rows)
    layer_out = jnp.einsum(
        "kwt,kwc->tkc", mixed_down, second_left, preferred_element_type=fp
    ).astype(bf)
    layer_out = layer_out.reshape(tok_rows, in_blocks * block_width)
    reduced = {}
    d_mixed_down = jnp.einsum(
        "tkc,kwc->kwt", cot_parts, second_left, preferred_element_type=fp
    ).astype(bf)
    d_mixed_down = d_mixed_down.reshape(in_blocks, all_hid, sub_width, tok_rows)
    d_down_inner = lax.all_to_all(d_mixed_down, "tensor", split_axis=1, concat_axis=0, tiled=True)
    d_hidden = jnp.einsum("kjgt,jbkg->jbt", d_down_inner, right_two, preferred_element_type=fp)
    d_pre = (d_hidden * gelu_slope(pre_piece)).astype(bf)
    d_mixed_up = jnp.einsum("jct,jbc->jbt", d_pre, first_left, preferred_element_type=fp).astype(bf)
    d_mixed_up = d_mixed_up.reshape(hid_blocks, all_in, sub_width, tok_rows)
    d_up_inner = lax.all_to_all(d_mixed_up, "tensor", split_axis=1, concat_axis=0, tiled=True)
    grad_tokens = jnp.einsum(
        "jkgt,kbjg->tkb", d_up_inner, right_one, preferred_element_type=fp
    ).astype(bf)
    grad_tokens = grad_tokens.reshape(tok_rows, in_blocks * block_width)
    d_up_flat = d_up_inner.reshape(all_hid * in_blocks * sub_width, tok_rows)
    tok_sorted = chunk_order(tok_parts[:, 0, :], 1, replicas)
    mixed_sorted = chunk_order(mixed_piece, 1, replicas)
    hidden_sorted = chunk_order(hidden, 1, replicas)
    down_sorted = chunk_order(mixed_down, 1, replicas)
    g_right_one = jnp.einsum("tb,nt->bn", tok_sorted, d_up_flat, preferred_element_type=fp)
    g_left_one = jnp.einsum("jbt,jct->jbc", mixed_sorted, d_pre, preferred_element_type=fp)
    g_right_two = jnp.einsum(
        "jbt,kjgt->jbkg", hidden_sorted, d_down_inner, preferred_element_type=fp
    ).reshape(hid_blocks, block_width, block_width)
    g_left_two = jnp.einsum("kwt,tkc->kwc", down_sorted, cot_parts, preferred_element_type=fp)

    def view(g):
        return g.reshape(in_blocks if g.ndim == 2 else g.shape[0], replicas, -1, g.shape[-1])

    reduced = dp_reduce_scatter(
        view(g_right_one), [view(g_left_one), view(g_right_two), view(g_left_two)], replicas
    )
    grad_right_one, grad_left_one, grad_right_two, grad_left_two = [r * grad_scale for r in reduced]
    return (layer_out, grad_tokens, grad_right_one, grad_left_one, grad_right_two, grad_left_two)


def solution(mesh):
    in_specs = (
        P("dp", "tensor"),
        P("tensor", None, None),
        P("tensor", None, None),
        P("tensor", None, None),
        P("tensor", None, None),
        P("dp", "tensor"),
    )
    out_specs = (
        P("dp", "tensor"),
        P("dp", "tensor"),
        P("tensor", "dp", None),
        P("tensor", "dp", None),
        P("tensor", "dp", None),
        P("tensor", "dp", None),
    )
    return jax.shard_map(shards, mesh=mesh, in_specs=in_specs, out_specs=out_specs, check_vma=False)
```

```python
import jax
import jax.numpy as jnp
from jax import lax
from jax.sharding import PartitionSpec as P

half_root = 0.7071067811865476
inv_root_two_pi = 0.3989422804014327


def gelu_value(value):
    return 0.5 * value * (1.0 + jax.scipy.special.erf(value * half_root))


def gelu_slope(value):
    return (
        0.5 * (1.0 + jax.scipy.special.erf(value * half_root))
        + value * jnp.exp(-0.5 * value * value) * inv_root_two_pi
    )


def dp_bit_order(replicas):
    bits = replicas.bit_length() - 1
    assert 1 << bits == replicas
    preferred = [0, 2, 3, 1]
    if bits == 4:
        return preferred
    return list(range(bits))


def chunk_order(x, axis, replicas):
    order = dp_bit_order(replicas)
    bits = len(order)
    shape = x.shape
    view = x.reshape(shape[:axis] + (2,) * bits + (shape[axis] // replicas,) + shape[axis + 1 :])
    moved = [axis + bits - 1 - b for b in order]
    perm = list(range(axis)) + moved + list(range(axis + bits, view.ndim))
    return jnp.transpose(view, perm).reshape(shape)


def dp_reduce_scatter(arrays, replicas):
    idx = lax.axis_index("dp")
    order = dp_bit_order(replicas)
    size = replicas
    for bit in order:
        half = size // 2
        me = (idx >> bit) & 1
        keeps = [lax.dynamic_slice_in_dim(a, me * half, half, axis=1) for a in arrays]
        sends = [lax.dynamic_slice_in_dim(a, (1 - me) * half, half, axis=1) for a in arrays]
        packed = jnp.concatenate([s.astype(jnp.bfloat16).reshape(-1, s.shape[-1]) for s in sends], axis=0)
        perm = [(i, i ^ (1 << bit)) for i in range(replicas)]
        got = lax.ppermute(packed, "dp", perm)
        arrays = []
        offset = 0
        for k in keeps:
            rows = k.size // k.shape[-1]
            arrays.append(k + got[offset : offset + rows].reshape(k.shape).astype(jnp.float32))
            offset += rows
        size = half
    return [a.reshape(a.shape[:1] + a.shape[2:]) for a in arrays]


def shards(tokens, first_right, first_left, second_right, second_left, cotangent):
    fp = jnp.float32
    bf = jnp.bfloat16
    tok_rows = tokens.shape[0]
    in_blocks = first_right.shape[0]
    block_width = first_right.shape[1]
    wide_width = first_right.shape[2]
    hid_blocks = first_left.shape[0]
    groups = lax.axis_size("tensor")
    replicas = lax.axis_size("dp")
    all_in = in_blocks * groups
    all_hid = hid_blocks * groups
    sub_width = wide_width // all_hid
    grad_scale = float(tok_rows * replicas) ** (-0.5)
    right_one = first_right.reshape(in_blocks, block_width, all_hid, sub_width)
    right_two = second_right.reshape(hid_blocks, block_width, all_in, sub_width)
    tok_parts = tokens.reshape(tok_rows, in_blocks, block_width)
    cot_parts = cotangent.reshape(tok_rows, in_blocks, block_width)

    up_inner = jnp.einsum("tkb,kbjg->jkgt", tok_parts, right_one, preferred_element_type=fp).astype(bf)
    d_mixed_down = jnp.einsum("tkc,kwc->kwt", cot_parts, second_left, preferred_element_type=fp).astype(bf)
    d_mixed_down = jnp.transpose(d_mixed_down.reshape(in_blocks, all_hid, sub_width, tok_rows), (1, 0, 2, 3))
    first_send = jnp.stack([up_inner, d_mixed_down], axis=1)
    first_got = lax.all_to_all(first_send, "tensor", split_axis=0, concat_axis=2, tiled=True)
    mixed_piece = first_got[:, 0].reshape(hid_blocks, block_width, tok_rows)
    d_down_inner = first_got[:, 1]

    pre_piece = jnp.einsum("jbt,jbc->jct", mixed_piece, first_left, preferred_element_type=fp)
    hidden = gelu_value(pre_piece).astype(bf)
    down_inner = jnp.einsum("jbt,jbkg->kjgt", hidden, right_two, preferred_element_type=fp).astype(bf)
    d_hidden = jnp.einsum("jkgt,jbkg->jbt", d_down_inner, right_two, preferred_element_type=fp)
    d_pre = (d_hidden * gelu_slope(pre_piece)).astype(bf)
    d_mixed_up = jnp.einsum("jct,jbc->jbt", d_pre, first_left, preferred_element_type=fp).astype(bf)
    d_mixed_up = jnp.transpose(d_mixed_up.reshape(hid_blocks, all_in, sub_width, tok_rows), (1, 0, 2, 3))

    second_send = jnp.stack([down_inner, d_mixed_up], axis=1)
    second_got = lax.all_to_all(second_send, "tensor", split_axis=0, concat_axis=2, tiled=True)
    mixed_down = second_got[:, 0].reshape(in_blocks, wide_width, tok_rows)
    d_up_inner = second_got[:, 1]

    layer_out = jnp.einsum("kwt,kwc->tkc", mixed_down, second_left, preferred_element_type=fp).astype(bf)
    layer_out = layer_out.reshape(tok_rows, in_blocks * block_width)
    grad_tokens = jnp.einsum("kjgt,kbjg->tkb", d_up_inner, right_one, preferred_element_type=fp).astype(bf)
    grad_tokens = grad_tokens.reshape(tok_rows, in_blocks * block_width)

    quarters = wide_width // block_width
    d_up_flat = d_up_inner.reshape(quarters, block_width, tok_rows)
    tok_sorted = chunk_order(tok_parts[:, 0, :], 1, replicas)
    tok_wide = jnp.broadcast_to(tok_sorted[None], (quarters,) + tok_sorted.shape)
    mixed_sorted = chunk_order(mixed_piece, 1, replicas)
    hidden_sorted = chunk_order(hidden, 1, replicas)
    down_sorted = chunk_order(mixed_down, 1, replicas)
    g_right_one = jnp.einsum("qtb,qnt->qbn", tok_wide, d_up_flat, preferred_element_type=fp)
    g_left_one = jnp.einsum("jbt,jct->jbc", mixed_sorted, d_pre, preferred_element_type=fp)
    g_right_two = jnp.einsum(
        "jbt,jkgt->jbkg", hidden_sorted, d_down_inner, preferred_element_type=fp
    ).reshape(hid_blocks, block_width, block_width)
    g_left_two = jnp.einsum("kwt,tkc->kwc", down_sorted, cot_parts, preferred_element_type=fp)

    def view(g):
        return g.reshape(g.shape[0], replicas, -1, g.shape[-1])

    reduced = dp_reduce_scatter(
        [view(g_right_one), view(g_left_one), view(g_right_two), view(g_left_two)], replicas
    )
    grad_right_one, grad_left_one, grad_right_two, grad_left_two = [r * grad_scale for r in reduced]
    grad_right_one = jnp.transpose(grad_right_one, (1, 0, 2)).reshape(in_blocks, -1, wide_width)
    return (layer_out, grad_tokens, grad_right_one, grad_left_one, grad_right_two, grad_left_two)


def solution(mesh):
    in_specs = (
        P("dp", "tensor"),
        P("tensor", None, None),
        P("tensor", None, None),
        P("tensor", None, None),
        P("tensor", None, None),
        P("dp", "tensor"),
    )
    out_specs = (
        P("dp", "tensor"),
        P("dp", "tensor"),
        P("tensor", "dp", None),
        P("tensor", "dp", None),
        P("tensor", "dp", None),
        P("tensor", "dp", None),
    )
    return jax.shard_map(shards, mesh=mesh, in_specs=in_specs, out_specs=out_specs, check_vma=False)
```

```python
import jax
import jax.numpy as jnp
from jax import lax
from jax.sharding import PartitionSpec as P

half_root = 0.7071067811865476
inv_root_two_pi = 0.3989422804014327


def gelu_value(value):
    return 0.5 * value * (1.0 + jax.scipy.special.erf(value * half_root))


def gelu_slope(value):
    return (
        0.5 * (1.0 + jax.scipy.special.erf(value * half_root))
        + value * jnp.exp(-0.5 * value * value) * inv_root_two_pi
    )


def dp_bit_order(replicas):
    bits = replicas.bit_length() - 1
    assert 1 << bits == replicas
    preferred = [0, 2, 3, 1]
    if bits == 4:
        return preferred
    return list(range(bits))


def chunk_order(x, axis, replicas):
    order = dp_bit_order(replicas)
    bits = len(order)
    shape = x.shape
    view = x.reshape(shape[:axis] + (2,) * bits + (shape[axis] // replicas,) + shape[axis + 1 :])
    moved = [axis + bits - 1 - b for b in order]
    perm = list(range(axis)) + moved + list(range(axis + bits, view.ndim))
    return jnp.transpose(view, perm).reshape(shape)


def dp_reduce_scatter(arrays, replicas):
    idx = lax.axis_index("dp")
    order = dp_bit_order(replicas)
    size = replicas
    for bit in order:
        half = size // 2
        me = (idx >> bit) & 1
        keeps = [lax.dynamic_slice_in_dim(a, me * half, half, axis=1) for a in arrays]
        sends = [lax.dynamic_slice_in_dim(a, (1 - me) * half, half, axis=1) for a in arrays]
        packed = jnp.concatenate([s.astype(jnp.bfloat16).reshape(-1, s.shape[-1]) for s in sends], axis=0)
        perm = [(i, i ^ (1 << bit)) for i in range(replicas)]
        got = lax.ppermute(packed, "dp", perm)
        arrays = []
        offset = 0
        for k in keeps:
            rows = k.size // k.shape[-1]
            arrays.append(k + got[offset : offset + rows].reshape(k.shape).astype(jnp.float32))
            offset += rows
        size = half
    return [a.reshape(a.shape[:1] + a.shape[2:]) for a in arrays]


def shards(tokens, first_right, first_left, second_right, second_left, cotangent):
    fp = jnp.float32
    bf = jnp.bfloat16
    tok_rows = tokens.shape[0]
    in_blocks = first_right.shape[0]
    block_width = first_right.shape[1]
    wide_width = first_right.shape[2]
    hid_blocks = first_left.shape[0]
    groups = lax.axis_size("tensor")
    replicas = lax.axis_size("dp")
    all_in = in_blocks * groups
    all_hid = hid_blocks * groups
    sub_width = wide_width // all_hid
    grad_scale = float(tok_rows * replicas) ** (-0.5)
    right_one = first_right.reshape(in_blocks, block_width, all_hid, sub_width)
    right_two = second_right.reshape(hid_blocks, block_width, all_in, sub_width)
    tok_parts = tokens.reshape(tok_rows, in_blocks, block_width)
    cot_parts = cotangent.reshape(tok_rows, in_blocks, block_width)
    up_inner = jnp.einsum("tkb,kbjg->jkgt", tok_parts, right_one, preferred_element_type=fp).astype(
        bf
    )
    arrived = lax.all_to_all(up_inner, "tensor", split_axis=0, concat_axis=1, tiled=True)
    mixed_piece = arrived.reshape(hid_blocks, block_width, arrived.shape[3])
    pre_piece = jnp.einsum("jbt,jbc->jct", mixed_piece, first_left, preferred_element_type=fp)
    hidden = gelu_value(pre_piece).astype(bf)
    down_inner = jnp.einsum("jbt,jbkg->kjgt", hidden, right_two, preferred_element_type=fp).astype(
        bf
    )
    mixed_down = lax.all_to_all(down_inner, "tensor", split_axis=0, concat_axis=1, tiled=True)
    mixed_down = mixed_down.reshape(in_blocks, wide_width, tok_rows)
    layer_out = jnp.einsum(
        "kwt,kwc->tkc", mixed_down, second_left, preferred_element_type=fp
    ).astype(bf)
    layer_out = layer_out.reshape(tok_rows, in_blocks * block_width)
    reduced = {}
    d_mixed_down = jnp.einsum(
        "tkc,kwc->kwt", cot_parts, second_left, preferred_element_type=fp
    ).astype(bf)
    d_mixed_down = d_mixed_down.reshape(in_blocks, all_hid, sub_width, tok_rows)
    d_down_inner = lax.all_to_all(d_mixed_down, "tensor", split_axis=1, concat_axis=0, tiled=True)
    d_hidden = jnp.einsum("kjgt,jbkg->jbt", d_down_inner, right_two, preferred_element_type=fp)
    d_pre = (d_hidden * gelu_slope(pre_piece)).astype(bf)
    d_mixed_up = jnp.einsum("jct,jbc->jbt", d_pre, first_left, preferred_element_type=fp).astype(bf)
    d_mixed_up = d_mixed_up.reshape(hid_blocks, all_in, sub_width, tok_rows)
    d_up_inner = lax.all_to_all(d_mixed_up, "tensor", split_axis=1, concat_axis=0, tiled=True)
    grad_tokens = jnp.einsum(
        "jkgt,kbjg->tkb", d_up_inner, right_one, preferred_element_type=fp
    ).astype(bf)
    grad_tokens = grad_tokens.reshape(tok_rows, in_blocks * block_width)
    d_up_flat = d_up_inner.reshape(all_hid * in_blocks * sub_width, tok_rows)
    tok_sorted = chunk_order(tok_parts[:, 0, :], 1, replicas)
    mixed_sorted = chunk_order(mixed_piece, 1, replicas)
    hidden_sorted = chunk_order(hidden, 1, replicas)
    down_sorted = chunk_order(mixed_down, 1, replicas)
    g_right_one = jnp.einsum("tb,nt->bn", tok_sorted, d_up_flat, preferred_element_type=fp)
    g_left_one = jnp.einsum("jbt,jct->jbc", mixed_sorted, d_pre, preferred_element_type=fp)
    g_right_two = jnp.einsum(
        "jbt,kjgt->jbkg", hidden_sorted, d_down_inner, preferred_element_type=fp
    ).reshape(hid_blocks, block_width, block_width)
    g_left_two = jnp.einsum("kwt,tkc->kwc", down_sorted, cot_parts, preferred_element_type=fp)

    def view(g):
        return g.reshape(in_blocks if g.ndim == 2 else g.shape[0], replicas, -1, g.shape[-1])

    (red_left_two,) = dp_reduce_scatter([view(g_left_two)], replicas)
    red_left_one, red_right_two = dp_reduce_scatter([view(g_left_one), view(g_right_two)], replicas)
    (red_right_one,) = dp_reduce_scatter([view(g_right_one)], replicas)
    reduced = (red_right_one, red_left_one, red_right_two, red_left_two)
    grad_right_one, grad_left_one, grad_right_two, grad_left_two = [r * grad_scale for r in reduced]
    return (layer_out, grad_tokens, grad_right_one, grad_left_one, grad_right_two, grad_left_two)


def solution(mesh):
    in_specs = (
        P("dp", "tensor"),
        P("tensor", None, None),
        P("tensor", None, None),
        P("tensor", None, None),
        P("tensor", None, None),
        P("dp", "tensor"),
    )
    out_specs = (
        P("dp", "tensor"),
        P("dp", "tensor"),
        P("tensor", "dp", None),
        P("tensor", "dp", None),
        P("tensor", "dp", None),
        P("tensor", "dp", None),
    )
    return jax.shard_map(shards, mesh=mesh, in_specs=in_specs, out_specs=out_specs, check_vma=False)
```

```python
import jax
import jax.numpy as jnp
from jax import lax
from jax.sharding import PartitionSpec as P

half_root = 0.7071067811865476
inv_root_two_pi = 0.3989422804014327


def gelu_value(value):
    return 0.5 * value * (1.0 + jax.scipy.special.erf(value * half_root))


def gelu_slope(value):
    return (
        0.5 * (1.0 + jax.scipy.special.erf(value * half_root))
        + value * jnp.exp(-0.5 * value * value) * inv_root_two_pi
    )


def dp_bit_order(replicas):
    bits = replicas.bit_length() - 1
    assert 1 << bits == replicas
    preferred = [0, 2, 3, 1]
    if bits == 4:
        return preferred
    return list(range(bits))


def chunk_order(x, axis, replicas):
    order = dp_bit_order(replicas)
    bits = len(order)
    shape = x.shape
    view = x.reshape(shape[:axis] + (2,) * bits + (shape[axis] // replicas,) + shape[axis + 1 :])
    moved = [axis + bits - 1 - b for b in order]
    perm = list(range(axis)) + moved + list(range(axis + bits, view.ndim))
    return jnp.transpose(view, perm).reshape(shape)


def dp_reduce_scatter(arrays, replicas):
    idx = lax.axis_index("dp")
    order = dp_bit_order(replicas)
    size = replicas
    for bit in order:
        half = size // 2
        me = (idx >> bit) & 1
        keeps = [lax.dynamic_slice_in_dim(a, me * half, half, axis=1) for a in arrays]
        sends = [lax.dynamic_slice_in_dim(a, (1 - me) * half, half, axis=1) for a in arrays]
        packed = jnp.concatenate([s.astype(jnp.bfloat16).reshape(-1, s.shape[-1]) for s in sends], axis=0)
        perm = [(i, i ^ (1 << bit)) for i in range(replicas)]
        got = lax.ppermute(packed, "dp", perm)
        arrays = []
        offset = 0
        for k in keeps:
            rows = k.size // k.shape[-1]
            arrays.append(k + got[offset : offset + rows].reshape(k.shape).astype(jnp.float32))
            offset += rows
        size = half
    return [a.reshape(a.shape[:1] + a.shape[2:]) for a in arrays]


def shards(tokens, first_right, first_left, second_right, second_left, cotangent):
    fp = jnp.float32
    bf = jnp.bfloat16
    tok_rows = tokens.shape[0]
    in_blocks = first_right.shape[0]
    block_width = first_right.shape[1]
    wide_width = first_right.shape[2]
    hid_blocks = first_left.shape[0]
    groups = lax.axis_size("tensor")
    replicas = lax.axis_size("dp")
    all_in = in_blocks * groups
    all_hid = hid_blocks * groups
    sub_width = wide_width // all_hid
    grad_scale = float(tok_rows * replicas) ** (-0.5)
    right_one = first_right.reshape(in_blocks, block_width, all_hid, sub_width)
    right_two = second_right.reshape(hid_blocks, block_width, all_in, sub_width)
    tok_parts = tokens.reshape(tok_rows, in_blocks, block_width)
    cot_parts = cotangent.reshape(tok_rows, in_blocks, block_width)
    up_inner = jnp.einsum("tkb,kbjg->jkgt", tok_parts, right_one, preferred_element_type=fp).astype(
        bf
    )
    arrived = lax.all_to_all(up_inner, "tensor", split_axis=0, concat_axis=1, tiled=True)
    mixed_piece = arrived.reshape(hid_blocks, block_width, arrived.shape[3])
    pre_piece = jnp.einsum("jbt,jbc->jct", mixed_piece, first_left, preferred_element_type=fp)
    hidden = gelu_value(pre_piece).astype(bf)
    down_inner = jnp.einsum("jbt,jbkg->kjgt", hidden, right_two, preferred_element_type=fp).astype(
        bf
    )
    mixed_down = lax.all_to_all(down_inner, "tensor", split_axis=0, concat_axis=1, tiled=True)
    mixed_down = mixed_down.reshape(in_blocks, wide_width, tok_rows)
    layer_out = jnp.einsum(
        "kwt,kwc->tkc", mixed_down, second_left, preferred_element_type=fp
    ).astype(bf)
    layer_out = layer_out.reshape(tok_rows, in_blocks * block_width)
    reduced = {}
    d_mixed_down = jnp.einsum(
        "tkc,kwc->kwt", cot_parts, second_left, preferred_element_type=fp
    ).astype(bf)
    d_mixed_down = d_mixed_down.reshape(in_blocks, all_hid, sub_width, tok_rows)
    d_down_inner = lax.all_to_all(d_mixed_down, "tensor", split_axis=1, concat_axis=0, tiled=True)
    d_hidden = jnp.einsum("kjgt,jbkg->jbt", d_down_inner, right_two, preferred_element_type=fp)
    d_pre = (d_hidden * gelu_slope(pre_piece)).astype(bf)
    d_mixed_up = jnp.einsum("jct,jbc->jbt", d_pre, first_left, preferred_element_type=fp).astype(bf)
    d_mixed_up = d_mixed_up.reshape(hid_blocks, all_in, sub_width, tok_rows)
    d_up_inner = lax.all_to_all(d_mixed_up, "tensor", split_axis=1, concat_axis=0, tiled=True)
    mixed_sorted = chunk_order(mixed_piece, 1, replicas)
    hidden_sorted = chunk_order(hidden, 1, replicas)
    down_sorted = chunk_order(mixed_down, 1, replicas)
    g_left_one = jnp.einsum("jbt,jct->jbc", mixed_sorted, d_pre, preferred_element_type=fp)
    g_right_two = jnp.einsum(
        "jbt,kjgt->jbkg", hidden_sorted, d_down_inner, preferred_element_type=fp
    ).reshape(hid_blocks, block_width, block_width)
    g_left_two = jnp.einsum("kwt,tkc->kwc", down_sorted, cot_parts, preferred_element_type=fp)

    def view(g):
        return g.reshape(in_blocks if g.ndim == 2 else g.shape[0], replicas, -1, g.shape[-1])

    early = dp_reduce_scatter([view(g_left_two), view(g_left_one), view(g_right_two)], replicas)
    d_up_inner, *early = lax.optimization_barrier((d_up_inner, *early))
    red_left_two, red_left_one, red_right_two = early

    grad_tokens = jnp.einsum(
        "jkgt,kbjg->tkb", d_up_inner, right_one, preferred_element_type=fp
    ).astype(bf)
    grad_tokens = grad_tokens.reshape(tok_rows, in_blocks * block_width)
    d_up_flat = d_up_inner.reshape(all_hid * in_blocks * sub_width, tok_rows)
    tok_sorted = chunk_order(tok_parts[:, 0, :], 1, replicas)
    g_right_one = jnp.einsum("tb,nt->bn", tok_sorted, d_up_flat, preferred_element_type=fp)
    (red_right_one,) = dp_reduce_scatter([view(g_right_one)], replicas)
    reduced = (red_right_one, red_left_one, red_right_two, red_left_two)
    grad_right_one, grad_left_one, grad_right_two, grad_left_two = [r * grad_scale for r in reduced]
    return (layer_out, grad_tokens, grad_right_one, grad_left_one, grad_right_two, grad_left_two)


def solution(mesh):
    in_specs = (
        P("dp", "tensor"),
        P("tensor", None, None),
        P("tensor", None, None),
        P("tensor", None, None),
        P("tensor", None, None),
        P("dp", "tensor"),
    )
    out_specs = (
        P("dp", "tensor"),
        P("dp", "tensor"),
        P("tensor", "dp", None),
        P("tensor", "dp", None),
        P("tensor", "dp", None),
        P("tensor", "dp", None),
    )
    return jax.shard_map(shards, mesh=mesh, in_specs=in_specs, out_specs=out_specs, check_vma=False)
```

```python
import jax
import jax.numpy as jnp
from jax import lax
from jax.sharding import PartitionSpec as P

half_root = 0.7071067811865476
inv_root_two_pi = 0.3989422804014327


def gelu_value(value):
    return 0.5 * value * (1.0 + jax.scipy.special.erf(value * half_root))


def gelu_slope(value):
    return (
        0.5 * (1.0 + jax.scipy.special.erf(value * half_root))
        + value * jnp.exp(-0.5 * value * value) * inv_root_two_pi
    )


def dp_bit_order(replicas):
    bits = replicas.bit_length() - 1
    assert 1 << bits == replicas
    preferred = [0, 2, 3, 1]
    if bits == 4:
        return preferred
    return list(range(bits))


def chunk_order(x, axis, replicas):
    order = dp_bit_order(replicas)
    bits = len(order)
    shape = x.shape
    view = x.reshape(shape[:axis] + (2,) * bits + (shape[axis] // replicas,) + shape[axis + 1 :])
    moved = [axis + bits - 1 - b for b in order]
    perm = list(range(axis)) + moved + list(range(axis + bits, view.ndim))
    return jnp.transpose(view, perm).reshape(shape)


def dp_reduce_scatter(wide, narrow, replicas):
    idx = lax.axis_index("dp")
    order = dp_bit_order(replicas)
    arrays = [wide] + list(narrow)
    size = replicas
    for bit in order:
        half = size // 2
        me = (idx >> bit) & 1
        keeps = [lax.dynamic_slice_in_dim(a, me * half, half, axis=1) for a in arrays]
        sends = [lax.dynamic_slice_in_dim(a, (1 - me) * half, half, axis=1) for a in arrays]
        sends = [s.astype(jnp.bfloat16) for s in sends]
        first = sends[0].reshape(-1, sends[0].shape[-1])
        rest = jnp.concatenate([s.reshape(-1, s.shape[-1]) for s in sends[1:]], axis=0)
        perm = [(i, i ^ (1 << bit)) for i in range(replicas)]
        got_first, got_rest = lax.ppermute((first, rest), "dp", perm)
        arrays = [keeps[0] + got_first.reshape(keeps[0].shape).astype(jnp.float32)]
        offset = 0
        for k in keeps[1:]:
            rows = k.size // k.shape[-1]
            part = got_rest[offset : offset + rows].reshape(k.shape)
            arrays.append(k + part.astype(jnp.float32))
            offset += rows
        size = half
    return [a.reshape(a.shape[:1] + a.shape[2:]) for a in arrays]


def shards(tokens, first_right, first_left, second_right, second_left, cotangent):
    fp = jnp.float32
    bf = jnp.bfloat16
    tok_rows = tokens.shape[0]
    in_blocks = first_right.shape[0]
    block_width = first_right.shape[1]
    wide_width = first_right.shape[2]
    hid_blocks = first_left.shape[0]
    groups = lax.axis_size("tensor")
    replicas = lax.axis_size("dp")
    all_in = in_blocks * groups
    all_hid = hid_blocks * groups
    sub_width = wide_width // all_hid
    grad_scale = float(tok_rows * replicas) ** (-0.5)
    right_one = first_right.reshape(in_blocks, block_width, all_hid, sub_width)
    right_two = second_right.reshape(hid_blocks, block_width, all_in, sub_width)
    tok_parts = tokens.reshape(tok_rows, in_blocks, block_width)
    cot_parts = cotangent.reshape(tok_rows, in_blocks, block_width)

    up_inner = jnp.einsum("tkb,kbjg->jkgt", tok_parts, right_one, preferred_element_type=fp).astype(bf)
    d_mixed_down = jnp.einsum("tkc,kwc->kwt", cot_parts, second_left, preferred_element_type=fp).astype(bf)
    d_mixed_down = jnp.transpose(d_mixed_down.reshape(in_blocks, all_hid, sub_width, tok_rows), (1, 0, 2, 3))
    first_send = jnp.stack([up_inner, d_mixed_down], axis=1)
    first_got = lax.all_to_all(first_send, "tensor", split_axis=0, concat_axis=2, tiled=True)
    mixed_piece = first_got[:, 0].reshape(hid_blocks, block_width, tok_rows)
    d_down_inner = first_got[:, 1]

    pre_piece = jnp.einsum("jbt,jbc->jct", mixed_piece, first_left, preferred_element_type=fp)
    hidden = gelu_value(pre_piece).astype(bf)
    down_inner = jnp.einsum("jbt,jbkg->kjgt", hidden, right_two, preferred_element_type=fp).astype(bf)
    d_hidden = jnp.einsum("jkgt,jbkg->jbt", d_down_inner, right_two, preferred_element_type=fp)
    d_pre = (d_hidden * gelu_slope(pre_piece)).astype(bf)
    d_mixed_up = jnp.einsum("jct,jbc->jbt", d_pre, first_left, preferred_element_type=fp).astype(bf)
    d_mixed_up = jnp.transpose(d_mixed_up.reshape(hid_blocks, all_in, sub_width, tok_rows), (1, 0, 2, 3))

    second_send = jnp.stack([down_inner, d_mixed_up], axis=1)
    second_got = lax.all_to_all(second_send, "tensor", split_axis=0, concat_axis=2, tiled=True)
    mixed_down = second_got[:, 0].reshape(in_blocks, wide_width, tok_rows)
    d_up_inner = second_got[:, 1]

    layer_out = jnp.einsum("kwt,kwc->tkc", mixed_down, second_left, preferred_element_type=fp).astype(bf)
    layer_out = layer_out.reshape(tok_rows, in_blocks * block_width)
    grad_tokens = jnp.einsum("kjgt,kbjg->tkb", d_up_inner, right_one, preferred_element_type=fp).astype(bf)
    grad_tokens = grad_tokens.reshape(tok_rows, in_blocks * block_width)

    d_up_flat = d_up_inner.reshape(all_hid * in_blocks * sub_width, tok_rows)
    tok_sorted = chunk_order(tok_parts[:, 0, :], 1, replicas)
    mixed_sorted = chunk_order(mixed_piece, 1, replicas)
    hidden_sorted = chunk_order(hidden, 1, replicas)
    down_sorted = chunk_order(mixed_down, 1, replicas)
    g_right_one = jnp.einsum("tb,nt->bn", tok_sorted, d_up_flat, preferred_element_type=fp)
    g_left_one = jnp.einsum("jbt,jct->jbc", mixed_sorted, d_pre, preferred_element_type=fp)
    g_right_two = jnp.einsum(
        "jbt,jkgt->jbkg", hidden_sorted, d_down_inner, preferred_element_type=fp
    ).reshape(hid_blocks, block_width, block_width)
    g_left_two = jnp.einsum("kwt,tkc->kwc", down_sorted, cot_parts, preferred_element_type=fp)

    def view(g):
        return g.reshape(in_blocks if g.ndim == 2 else g.shape[0], replicas, -1, g.shape[-1])

    reduced = dp_reduce_scatter(
        view(g_right_one), [view(g_left_one), view(g_right_two), view(g_left_two)], replicas
    )
    grad_right_one, grad_left_one, grad_right_two, grad_left_two = [r * grad_scale for r in reduced]
    return (layer_out, grad_tokens, grad_right_one, grad_left_one, grad_right_two, grad_left_two)


def solution(mesh):
    in_specs = (
        P("dp", "tensor"),
        P("tensor", None, None),
        P("tensor", None, None),
        P("tensor", None, None),
        P("tensor", None, None),
        P("dp", "tensor"),
    )
    out_specs = (
        P("dp", "tensor"),
        P("dp", "tensor"),
        P("tensor", "dp", None),
        P("tensor", "dp", None),
        P("tensor", "dp", None),
        P("tensor", "dp", None),
    )
    return jax.shard_map(shards, mesh=mesh, in_specs=in_specs, out_specs=out_specs, check_vma=False)
```

```python
import jax
import jax.numpy as jnp
from jax import lax
from jax.sharding import PartitionSpec as P


half_root = 0.7071067811865476
inv_root_two_pi = 0.3989422804014327


def gelu_value(value):
    return 0.5 * value * (1.0 + jax.scipy.special.erf(value * half_root))


def gelu_slope(value):
    return (
        0.5 * (1.0 + jax.scipy.special.erf(value * half_root))
        + value * jnp.exp(-0.5 * value * value) * inv_root_two_pi
    )


def dp_bit_order(replicas):
    bits = replicas.bit_length() - 1
    assert 1 << bits == replicas
    preferred = [0, 2, 3, 1]
    if bits == 4:
        return preferred
    return list(range(bits))


def chunk_order(x, axis, replicas):
    order = dp_bit_order(replicas)
    bits = len(order)
    shape = x.shape
    view = x.reshape(shape[:axis] + (2,) * bits + (shape[axis] // replicas,) + shape[axis + 1 :])
    moved = [axis + bits - 1 - b for b in order]
    perm = list(range(axis)) + moved + list(range(axis + bits, view.ndim))
    return jnp.transpose(view, perm).reshape(shape)


def dp_reduce_scatter(arrays, replicas, first=0, last=None):
    idx = lax.axis_index("dp")
    order = dp_bit_order(replicas)
    last = len(order) if last is None else last
    size = replicas >> first
    for bit in order[first:last]:
        half = size // 2
        me = (idx >> bit) & 1
        keeps = [lax.dynamic_slice_in_dim(a, me * half, half, axis=1) for a in arrays]
        sends = [lax.dynamic_slice_in_dim(a, (1 - me) * half, half, axis=1) for a in arrays]
        packed = jnp.concatenate([s.astype(jnp.bfloat16).reshape(-1, s.shape[-1]) for s in sends], axis=0)
        perm = [(i, i ^ (1 << bit)) for i in range(replicas)]
        got = lax.ppermute(packed, "dp", perm)
        arrays = []
        offset = 0
        for k in keeps:
            rows = k.size // k.shape[-1]
            arrays.append(k + got[offset : offset + rows].reshape(k.shape).astype(jnp.float32))
            offset += rows
        size = half
    return arrays


def layer(tokens, first_right, first_left, second_right, second_left, cotangent):
    fp = jnp.float32
    bf = jnp.bfloat16
    tok_rows = tokens.shape[0]
    in_blocks = first_right.shape[0]
    block_width = first_right.shape[1]
    wide_width = first_right.shape[2]
    hid_blocks = first_left.shape[0]
    groups = lax.axis_size("tensor")
    replicas = lax.axis_size("dp")
    all_in = in_blocks * groups
    all_hid = hid_blocks * groups
    sub_width = wide_width // all_hid
    grad_scale = float(tok_rows * replicas) ** (-0.5)
    right_one = first_right.reshape(in_blocks, block_width, all_hid, sub_width)
    right_two = second_right.reshape(hid_blocks, block_width, all_in, sub_width)
    tok_parts = tokens.reshape(tok_rows, in_blocks, block_width)
    cot_parts = cotangent.reshape(tok_rows, in_blocks, block_width)
    up_inner = jnp.einsum("tkb,kbjg->jkgt", tok_parts, right_one, preferred_element_type=fp).astype(
        bf
    )
    arrived = lax.all_to_all(up_inner, "tensor", split_axis=0, concat_axis=1, tiled=True)
    mixed_piece = arrived.reshape(hid_blocks, block_width, arrived.shape[3])
    pre_piece = jnp.einsum("jbt,jbc->jct", mixed_piece, first_left, preferred_element_type=fp)
    hidden = gelu_value(pre_piece).astype(bf)
    down_inner = jnp.einsum("jbt,jbkg->kjgt", hidden, right_two, preferred_element_type=fp).astype(
        bf
    )
    mixed_down = lax.all_to_all(down_inner, "tensor", split_axis=0, concat_axis=1, tiled=True)
    mixed_down = mixed_down.reshape(in_blocks, wide_width, tok_rows)
    layer_out = jnp.einsum(
        "kwt,kwc->tkc", mixed_down, second_left, preferred_element_type=fp
    ).astype(bf)
    layer_out = layer_out.reshape(tok_rows, in_blocks * block_width)
    reduced = {}
    d_mixed_down = jnp.einsum(
        "tkc,kwc->kwt", cot_parts, second_left, preferred_element_type=fp
    ).astype(bf)
    d_mixed_down = d_mixed_down.reshape(in_blocks, all_hid, sub_width, tok_rows)
    d_down_inner = lax.all_to_all(d_mixed_down, "tensor", split_axis=1, concat_axis=0, tiled=True)
    d_hidden = jnp.einsum("kjgt,jbkg->jbt", d_down_inner, right_two, preferred_element_type=fp)
    d_pre = (d_hidden * gelu_slope(pre_piece)).astype(bf)
    d_mixed_up = jnp.einsum("jct,jbc->jbt", d_pre, first_left, preferred_element_type=fp).astype(bf)
    d_mixed_up = d_mixed_up.reshape(hid_blocks, all_in, sub_width, tok_rows)
    d_up_inner = lax.all_to_all(d_mixed_up, "tensor", split_axis=1, concat_axis=0, tiled=True)
    mixed_sorted = chunk_order(mixed_piece, 1, replicas)
    hidden_sorted = chunk_order(hidden, 1, replicas)
    down_sorted = chunk_order(mixed_down, 1, replicas)
    g_left_one = jnp.einsum("jbt,jct->jbc", mixed_sorted, d_pre, preferred_element_type=fp)
    g_right_two = jnp.einsum(
        "jbt,kjgt->jbkg", hidden_sorted, d_down_inner, preferred_element_type=fp
    ).reshape(hid_blocks, block_width, block_width)
    g_left_two = jnp.einsum("kwt,tkc->kwc", down_sorted, cot_parts, preferred_element_type=fp)

    def view(g):
        return g.reshape(in_blocks if g.ndim == 2 else g.shape[0], replicas, -1, g.shape[-1])

    early_stages = 2
    early = dp_reduce_scatter(
        [view(g_left_two), view(g_left_one), view(g_right_two)], replicas, 0, early_stages
    )
    d_up_inner, *early = lax.optimization_barrier((d_up_inner, *early))

    grad_tokens = jnp.einsum(
        "jkgt,kbjg->tkb", d_up_inner, right_one, preferred_element_type=fp
    ).astype(bf)
    grad_tokens = grad_tokens.reshape(tok_rows, in_blocks * block_width)
    d_up_flat = d_up_inner.reshape(all_hid * in_blocks * sub_width, tok_rows)
    tok_sorted = chunk_order(tok_parts[:, 0, :], 1, replicas)
    g_right_one = jnp.einsum("tb,nt->bn", tok_sorted, d_up_flat, preferred_element_type=fp)
    late = [view(g_right_one)]
    stages = len(dp_bit_order(replicas))
    for stage in range(stages):
        late = dp_reduce_scatter(late, replicas, stage, stage + 1)
        if early_stages + stage < stages:
            early = dp_reduce_scatter(early, replicas, early_stages + stage, early_stages + stage + 1)
    red_right_one = late[0][:, 0]
    red_left_two, red_left_one, red_right_two = [e[:, 0] for e in early]
    reduced = (red_right_one, red_left_one, red_right_two, red_left_two)
    grad_right_one, grad_left_one, grad_right_two, grad_left_two = [r * grad_scale for r in reduced]
    return (layer_out, grad_tokens, grad_right_one, grad_left_one, grad_right_two, grad_left_two)


def solution(mesh):
    in_specs = (
        P("dp", "tensor"),
        P("tensor", None, None),
        P("tensor", None, None),
        P("tensor", None, None),
        P("tensor", None, None),
        P("dp", "tensor"),
    )
    out_specs = (
        P("dp", "tensor"),
        P("dp", "tensor"),
        P("tensor", "dp", None),
        P("tensor", "dp", None),
        P("tensor", "dp", None),
        P("tensor", "dp", None),
    )
    return jax.shard_map(layer, mesh=mesh, in_specs=in_specs, out_specs=out_specs, check_vma=False)
```

```python
import jax
import jax.numpy as jnp
from jax import lax
from jax.sharding import PartitionSpec as P


half_root = 0.7071067811865476
inv_root_two_pi = 0.3989422804014327


def gelu_value(value):
    return 0.5 * value * (1.0 + jax.scipy.special.erf(value * half_root))


def gelu_slope(value):
    return (
        0.5 * (1.0 + jax.scipy.special.erf(value * half_root))
        + value * jnp.exp(-0.5 * value * value) * inv_root_two_pi
    )


def dp_bit_order(replicas):
    bits = replicas.bit_length() - 1
    assert 1 << bits == replicas
    preferred = [0, 2, 3, 1]
    if bits == 4:
        return preferred
    return list(range(bits))


def chunk_order(x, axis, replicas):
    order = dp_bit_order(replicas)
    bits = len(order)
    shape = x.shape
    view = x.reshape(shape[:axis] + (2,) * bits + (shape[axis] // replicas,) + shape[axis + 1 :])
    moved = [axis + bits - 1 - b for b in order]
    perm = list(range(axis)) + moved + list(range(axis + bits, view.ndim))
    return jnp.transpose(view, perm).reshape(shape)


def dp_reduce_scatter(arrays, replicas, first=0, last=None):
    idx = lax.axis_index("dp")
    order = dp_bit_order(replicas)
    last = len(order) if last is None else last
    size = replicas >> first
    for bit in order[first:last]:
        half = size // 2
        me = (idx >> bit) & 1
        keeps = [lax.dynamic_slice_in_dim(a, me * half, half, axis=1) for a in arrays]
        sends = [lax.dynamic_slice_in_dim(a, (1 - me) * half, half, axis=1) for a in arrays]
        packed = jnp.concatenate([s.astype(jnp.bfloat16).reshape(-1, s.shape[-1]) for s in sends], axis=0)
        perm = [(i, i ^ (1 << bit)) for i in range(replicas)]
        got = lax.ppermute(packed, "dp", perm)
        arrays = []
        offset = 0
        for k in keeps:
            rows = k.size // k.shape[-1]
            arrays.append(k + got[offset : offset + rows].reshape(k.shape).astype(jnp.float32))
            offset += rows
        size = half
    return arrays


def layer(tokens, first_right, first_left, second_right, second_left, cotangent):
    fp = jnp.float32
    bf = jnp.bfloat16
    tok_rows = tokens.shape[0]
    in_blocks = first_right.shape[0]
    block_width = first_right.shape[1]
    wide_width = first_right.shape[2]
    hid_blocks = first_left.shape[0]
    groups = lax.axis_size("tensor")
    replicas = lax.axis_size("dp")
    all_in = in_blocks * groups
    all_hid = hid_blocks * groups
    sub_width = wide_width // all_hid
    grad_scale = float(tok_rows * replicas) ** (-0.5)
    right_one = first_right.reshape(in_blocks, block_width, all_hid, sub_width)
    right_two = second_right.reshape(hid_blocks, block_width, all_in, sub_width)
    tok_parts = tokens.reshape(tok_rows, in_blocks, block_width)
    cot_parts = cotangent.reshape(tok_rows, in_blocks, block_width)
    up_inner = jnp.einsum("tkb,kbjg->jkgt", tok_parts, right_one, preferred_element_type=fp).astype(
        bf
    )
    arrived = lax.all_to_all(up_inner, "tensor", split_axis=0, concat_axis=1, tiled=True)
    mixed_piece = arrived.reshape(hid_blocks, block_width, arrived.shape[3])
    pre_piece = jnp.einsum("jbt,jbc->jct", mixed_piece, first_left, preferred_element_type=fp)
    hidden = gelu_value(pre_piece).astype(bf)
    down_inner = jnp.einsum("jbt,jbkg->kjgt", hidden, right_two, preferred_element_type=fp).astype(
        bf
    )
    mixed_down = lax.all_to_all(down_inner, "tensor", split_axis=0, concat_axis=1, tiled=True)
    mixed_down = mixed_down.reshape(in_blocks, wide_width, tok_rows)
    layer_out = jnp.einsum(
        "kwt,kwc->tkc", mixed_down, second_left, preferred_element_type=fp
    ).astype(bf)
    layer_out = layer_out.reshape(tok_rows, in_blocks * block_width)
    reduced = {}
    d_mixed_down = jnp.einsum(
        "tkc,kwc->kwt", cot_parts, second_left, preferred_element_type=fp
    ).astype(bf)
    d_mixed_down = d_mixed_down.reshape(in_blocks, all_hid, sub_width, tok_rows)
    d_down_inner = lax.all_to_all(d_mixed_down, "tensor", split_axis=1, concat_axis=0, tiled=True)

    def view(g):
        return g.reshape(in_blocks if g.ndim == 2 else g.shape[0], replicas, -1, g.shape[-1])

    down_sorted = chunk_order(mixed_down, 1, replicas)
    g_left_two = jnp.einsum("kwt,tkc->kwc", down_sorted, cot_parts, preferred_element_type=fp)
    (mid,) = dp_reduce_scatter([view(g_left_two)], replicas)
    d_down_inner, mid = lax.optimization_barrier((d_down_inner, mid))
    red_left_two = mid[:, 0]
    d_hidden = jnp.einsum("kjgt,jbkg->jbt", d_down_inner, right_two, preferred_element_type=fp)
    d_pre = (d_hidden * gelu_slope(pre_piece)).astype(bf)
    d_mixed_up = jnp.einsum("jct,jbc->jbt", d_pre, first_left, preferred_element_type=fp).astype(bf)
    d_mixed_up = d_mixed_up.reshape(hid_blocks, all_in, sub_width, tok_rows)
    d_up_inner = lax.all_to_all(d_mixed_up, "tensor", split_axis=1, concat_axis=0, tiled=True)
    mixed_sorted = chunk_order(mixed_piece, 1, replicas)
    hidden_sorted = chunk_order(hidden, 1, replicas)
    g_left_one = jnp.einsum("jbt,jct->jbc", mixed_sorted, d_pre, preferred_element_type=fp)
    d_down_rows = jnp.transpose(d_down_inner, (1, 0, 2, 3)).reshape(hid_blocks, all_in * sub_width, tok_rows)
    g_right_two = jnp.einsum("jbt,jnt->jbn", hidden_sorted, d_down_rows, preferred_element_type=fp)

    early_stages = 2
    early = dp_reduce_scatter(
        [view(g_left_one), view(g_right_two)], replicas, 0, early_stages
    )
    d_up_inner, *early = lax.optimization_barrier((d_up_inner, *early))

    grad_tokens = jnp.einsum(
        "jkgt,kbjg->tkb", d_up_inner, right_one, preferred_element_type=fp
    ).astype(bf)
    grad_tokens = grad_tokens.reshape(tok_rows, in_blocks * block_width)
    d_up_flat = d_up_inner.reshape(all_hid * in_blocks * sub_width, tok_rows)
    tok_sorted = chunk_order(tok_parts[:, 0, :], 1, replicas)
    g_right_one = jnp.einsum("tb,nt->bn", tok_sorted, d_up_flat, preferred_element_type=fp)
    late = [view(g_right_one)]
    stages = len(dp_bit_order(replicas))
    for stage in range(stages):
        late = dp_reduce_scatter(late, replicas, stage, stage + 1)
        if early_stages + stage < stages:
            early = dp_reduce_scatter(early, replicas, early_stages + stage, early_stages + stage + 1)
    red_right_one = late[0][:, 0]
    red_left_one, red_right_two = [e[:, 0] for e in early]
    reduced = (red_right_one, red_left_one, red_right_two, red_left_two)
    grad_right_one, grad_left_one, grad_right_two, grad_left_two = [r * grad_scale for r in reduced]
    return (layer_out, grad_tokens, grad_right_one, grad_left_one, grad_right_two, grad_left_two)


def solution(mesh):
    in_specs = (
        P("dp", "tensor"),
        P("tensor", None, None),
        P("tensor", None, None),
        P("tensor", None, None),
        P("tensor", None, None),
        P("dp", "tensor"),
    )
    out_specs = (
        P("dp", "tensor"),
        P("dp", "tensor"),
        P("tensor", "dp", None),
        P("tensor", "dp", None),
        P("tensor", "dp", None),
        P("tensor", "dp", None),
    )
    return jax.shard_map(layer, mesh=mesh, in_specs=in_specs, out_specs=out_specs, check_vma=False)
```

```python
import jax
import jax.numpy as jnp
from jax import lax
from jax.sharding import PartitionSpec as P


half_root = 0.7071067811865476
inv_root_two_pi = 0.3989422804014327


def gelu_value(value):
    return 0.5 * value * (1.0 + jax.scipy.special.erf(value * half_root))


def gelu_slope(value):
    return (
        0.5 * (1.0 + jax.scipy.special.erf(value * half_root))
        + value * jnp.exp(-0.5 * value * value) * inv_root_two_pi
    )


def dp_bit_order(replicas):
    bits = replicas.bit_length() - 1
    assert 1 << bits == replicas
    preferred = [0, 2, 3, 1]
    if bits == 4:
        return preferred
    return list(range(bits))


def chunk_order(x, axis, replicas):
    order = dp_bit_order(replicas)
    bits = len(order)
    shape = x.shape
    view = x.reshape(shape[:axis] + (2,) * bits + (shape[axis] // replicas,) + shape[axis + 1 :])
    moved = [axis + bits - 1 - b for b in order]
    perm = list(range(axis)) + moved + list(range(axis + bits, view.ndim))
    return jnp.transpose(view, perm).reshape(shape)


def dp_reduce_scatter(arrays, replicas, first=0, last=None):
    idx = lax.axis_index("dp")
    order = dp_bit_order(replicas)
    last = len(order) if last is None else last
    size = replicas >> first
    for bit in order[first:last]:
        half = size // 2
        me = (idx >> bit) & 1
        keeps = [lax.dynamic_slice_in_dim(a, me * half, half, axis=1) for a in arrays]
        sends = [lax.dynamic_slice_in_dim(a, (1 - me) * half, half, axis=1) for a in arrays]
        packed = jnp.concatenate([s.astype(jnp.bfloat16).reshape(-1, s.shape[-1]) for s in sends], axis=0)
        perm = [(i, i ^ (1 << bit)) for i in range(replicas)]
        got = lax.ppermute(packed, "dp", perm)
        arrays = []
        offset = 0
        for k in keeps:
            rows = k.size // k.shape[-1]
            arrays.append(k + got[offset : offset + rows].reshape(k.shape).astype(jnp.float32))
            offset += rows
        size = half
    return arrays


def layer(tokens, first_right, first_left, second_right, second_left, cotangent):
    fp = jnp.float32
    bf = jnp.bfloat16
    tok_rows = tokens.shape[0]
    in_blocks = first_right.shape[0]
    block_width = first_right.shape[1]
    wide_width = first_right.shape[2]
    hid_blocks = first_left.shape[0]
    groups = lax.axis_size("tensor")
    replicas = lax.axis_size("dp")
    all_in = in_blocks * groups
    all_hid = hid_blocks * groups
    sub_width = wide_width // all_hid
    grad_scale = float(tok_rows * replicas) ** (-0.5)
    right_one = first_right.reshape(in_blocks, block_width, all_hid, sub_width)
    right_two = second_right.reshape(hid_blocks, block_width, all_in, sub_width)
    tok_parts = tokens.reshape(tok_rows, in_blocks, block_width)
    cot_parts = cotangent.reshape(tok_rows, in_blocks, block_width)
    up_inner = jnp.einsum("tkb,kbjg->jkgt", tok_parts, right_one, preferred_element_type=fp).astype(
        bf
    )
    arrived = lax.all_to_all(up_inner, "tensor", split_axis=0, concat_axis=1, tiled=True)
    mixed_piece = arrived.reshape(hid_blocks, block_width, arrived.shape[3])
    pre_piece = jnp.einsum("jbt,jbc->jct", mixed_piece, first_left, preferred_element_type=fp)
    hidden = gelu_value(pre_piece).astype(bf)
    down_inner = jnp.einsum("jbt,jbkg->kjgt", hidden, right_two, preferred_element_type=fp).astype(
        bf
    )
    mixed_down = lax.all_to_all(down_inner, "tensor", split_axis=0, concat_axis=1, tiled=True)
    mixed_down = mixed_down.reshape(in_blocks, wide_width, tok_rows)
    layer_out = jnp.einsum(
        "kwt,kwc->tkc", mixed_down, second_left, preferred_element_type=fp
    ).astype(bf)
    layer_out = layer_out.reshape(tok_rows, in_blocks * block_width)
    reduced = {}
    d_mixed_down = jnp.einsum(
        "tkc,kwc->kwt", cot_parts, second_left, preferred_element_type=fp
    ).astype(bf)
    d_mixed_down = d_mixed_down.reshape(in_blocks, all_hid, sub_width, tok_rows)
    d_down_inner = lax.all_to_all(d_mixed_down, "tensor", split_axis=1, concat_axis=0, tiled=True)
    d_hidden = jnp.einsum("kjgt,jbkg->jbt", d_down_inner, right_two, preferred_element_type=fp)
    d_pre = (d_hidden * gelu_slope(pre_piece)).astype(bf)
    d_mixed_up = jnp.einsum("jct,jbc->jbt", d_pre, first_left, preferred_element_type=fp).astype(bf)
    d_mixed_up = d_mixed_up.reshape(hid_blocks, all_in, sub_width, tok_rows)
    d_up_inner = lax.all_to_all(d_mixed_up, "tensor", split_axis=1, concat_axis=0, tiled=True)
    mixed_sorted = chunk_order(mixed_piece, 1, replicas)
    hidden_sorted = chunk_order(hidden, 1, replicas)
    down_sorted = chunk_order(mixed_down, 1, replicas)
    g_left_one = jnp.einsum("jbt,jct->jbc", mixed_sorted, d_pre, preferred_element_type=fp)
    d_down_rows = jnp.transpose(d_down_inner, (1, 0, 2, 3)).reshape(hid_blocks, all_in * sub_width, tok_rows)
    g_right_two = jnp.einsum("jbt,jnt->jbn", hidden_sorted, d_down_rows, preferred_element_type=fp)
    g_left_two = jnp.einsum("kwt,tkc->kwc", down_sorted, cot_parts, preferred_element_type=fp)

    def view(g):
        return g.reshape(in_blocks if g.ndim == 2 else g.shape[0], replicas, -1, g.shape[-1])

    early_stages = 3
    early = dp_reduce_scatter(
        [view(g_left_two), view(g_left_one), view(g_right_two)], replicas, 0, early_stages
    )
    d_up_inner, *early = lax.optimization_barrier((d_up_inner, *early))

    grad_tokens = jnp.einsum(
        "jkgt,kbjg->tkb", d_up_inner, right_one, preferred_element_type=fp
    ).astype(bf)
    grad_tokens = grad_tokens.reshape(tok_rows, in_blocks * block_width)
    d_up_flat = d_up_inner.reshape(all_hid * in_blocks * sub_width, tok_rows)
    tok_sorted = chunk_order(tok_parts[:, 0, :], 1, replicas)
    g_right_one = jnp.einsum("tb,nt->bn", tok_sorted, d_up_flat, preferred_element_type=fp)
    late = [view(g_right_one)]
    stages = len(dp_bit_order(replicas))
    for stage in range(stages):
        late = dp_reduce_scatter(late, replicas, stage, stage + 1)
        if early_stages + stage < stages:
            early = dp_reduce_scatter(early, replicas, early_stages + stage, early_stages + stage + 1)
    red_right_one = late[0][:, 0]
    red_left_two, red_left_one, red_right_two = [e[:, 0] for e in early]
    reduced = (red_right_one, red_left_one, red_right_two, red_left_two)
    grad_right_one, grad_left_one, grad_right_two, grad_left_two = [r * grad_scale for r in reduced]
    return (layer_out, grad_tokens, grad_right_one, grad_left_one, grad_right_two, grad_left_two)


def solution(mesh):
    in_specs = (
        P("dp", "tensor"),
        P("tensor", None, None),
        P("tensor", None, None),
        P("tensor", None, None),
        P("tensor", None, None),
        P("dp", "tensor"),
    )
    out_specs = (
        P("dp", "tensor"),
        P("dp", "tensor"),
        P("tensor", "dp", None),
        P("tensor", "dp", None),
        P("tensor", "dp", None),
        P("tensor", "dp", None),
    )
    return jax.shard_map(layer, mesh=mesh, in_specs=in_specs, out_specs=out_specs, check_vma=False)
```

```python
import jax
import jax.numpy as jnp
from jax import lax
from jax.sharding import PartitionSpec as P


half_root = 0.7071067811865476
inv_root_two_pi = 0.3989422804014327


def gelu_value(value):
    return 0.5 * value * (1.0 + jax.scipy.special.erf(value * half_root))


def gelu_slope(value):
    return (
        0.5 * (1.0 + jax.scipy.special.erf(value * half_root))
        + value * jnp.exp(-0.5 * value * value) * inv_root_two_pi
    )


def dp_bit_order(replicas):
    bits = replicas.bit_length() - 1
    assert 1 << bits == replicas
    preferred = [0, 2, 3, 1]
    if bits == 4:
        return preferred
    return list(range(bits))


def chunk_order(x, axis, replicas):
    order = dp_bit_order(replicas)
    bits = len(order)
    shape = x.shape
    view = x.reshape(shape[:axis] + (2,) * bits + (shape[axis] // replicas,) + shape[axis + 1 :])
    moved = [axis + bits - 1 - b for b in order]
    perm = list(range(axis)) + moved + list(range(axis + bits, view.ndim))
    return jnp.transpose(view, perm).reshape(shape)


def dp_reduce_scatter(arrays, replicas, first=0, last=None):
    idx = lax.axis_index("dp")
    order = dp_bit_order(replicas)
    last = len(order) if last is None else last
    size = replicas >> first
    for bit in order[first:last]:
        half = size // 2
        me = (idx >> bit) & 1
        keeps = [lax.dynamic_slice_in_dim(a, me * half, half, axis=1) for a in arrays]
        sends = [lax.dynamic_slice_in_dim(a, (1 - me) * half, half, axis=1) for a in arrays]
        packed = jnp.concatenate([s.astype(jnp.bfloat16).reshape(-1, s.shape[-1]) for s in sends], axis=0)
        perm = [(i, i ^ (1 << bit)) for i in range(replicas)]
        got = lax.ppermute(packed, "dp", perm)
        arrays = []
        offset = 0
        for k in keeps:
            rows = k.size // k.shape[-1]
            arrays.append(k + got[offset : offset + rows].reshape(k.shape).astype(jnp.float32))
            offset += rows
        size = half
    return arrays


def layer(tokens, first_right, first_left, second_right, second_left, cotangent):
    fp = jnp.float32
    bf = jnp.bfloat16
    tok_rows = tokens.shape[0]
    in_blocks = first_right.shape[0]
    block_width = first_right.shape[1]
    wide_width = first_right.shape[2]
    hid_blocks = first_left.shape[0]
    groups = lax.axis_size("tensor")
    replicas = lax.axis_size("dp")
    all_in = in_blocks * groups
    all_hid = hid_blocks * groups
    sub_width = wide_width // all_hid
    grad_scale = float(tok_rows * replicas) ** (-0.5)
    right_one = first_right.reshape(in_blocks, block_width, all_hid, sub_width)
    right_two = second_right.reshape(hid_blocks, block_width, all_in, sub_width)
    tok_parts = tokens.reshape(tok_rows, in_blocks, block_width)
    cot_parts = cotangent.reshape(tok_rows, in_blocks, block_width)
    up_inner = jnp.einsum("tkb,kbjg->jkgt", tok_parts, right_one, preferred_element_type=fp).astype(
        bf
    )
    arrived = lax.all_to_all(up_inner, "tensor", split_axis=0, concat_axis=1, tiled=True)
    mixed_piece = arrived.reshape(hid_blocks, block_width, arrived.shape[3])
    pre_piece = jnp.einsum("jbt,jbc->jct", mixed_piece, first_left, preferred_element_type=fp)
    hidden = gelu_value(pre_piece).astype(bf)
    down_inner = jnp.einsum("jbt,jbkg->kjgt", hidden, right_two, preferred_element_type=fp).astype(
        bf
    )
    mixed_down = lax.all_to_all(down_inner, "tensor", split_axis=0, concat_axis=1, tiled=True)
    mixed_down = mixed_down.reshape(in_blocks, wide_width, tok_rows)
    layer_out = jnp.einsum(
        "kwt,kwc->tkc", mixed_down, second_left, preferred_element_type=fp
    ).astype(bf)
    layer_out = layer_out.reshape(tok_rows, in_blocks * block_width)
    reduced = {}
    d_mixed_down = jnp.einsum(
        "tkc,kwc->kwt", cot_parts, second_left, preferred_element_type=fp
    ).astype(bf)
    d_mixed_down = d_mixed_down.reshape(in_blocks, all_hid, sub_width, tok_rows)
    d_down_inner = lax.all_to_all(d_mixed_down, "tensor", split_axis=1, concat_axis=0, tiled=True)

    def view(g):
        return g.reshape(in_blocks if g.ndim == 2 else g.shape[0], replicas, -1, g.shape[-1])

    down_sorted = chunk_order(mixed_down, 1, replicas)
    g_left_two = jnp.einsum("kwt,tkc->kwc", down_sorted, cot_parts, preferred_element_type=fp)
    mid = dp_reduce_scatter([view(g_left_two)], replicas, 0, 2)
    d_down_inner, *mid = lax.optimization_barrier((d_down_inner, *mid))
    d_hidden = jnp.einsum("kjgt,jbkg->jbt", d_down_inner, right_two, preferred_element_type=fp)
    d_pre = (d_hidden * gelu_slope(pre_piece)).astype(bf)
    d_mixed_up = jnp.einsum("jct,jbc->jbt", d_pre, first_left, preferred_element_type=fp).astype(bf)
    d_mixed_up = d_mixed_up.reshape(hid_blocks, all_in, sub_width, tok_rows)
    d_up_inner = lax.all_to_all(d_mixed_up, "tensor", split_axis=1, concat_axis=0, tiled=True)
    mixed_sorted = chunk_order(mixed_piece, 1, replicas)
    hidden_sorted = chunk_order(hidden, 1, replicas)
    g_left_one = jnp.einsum("jbt,jct->jbc", mixed_sorted, d_pre, preferred_element_type=fp)
    d_down_rows = jnp.transpose(d_down_inner, (1, 0, 2, 3)).reshape(hid_blocks, all_in * sub_width, tok_rows)
    g_right_two = jnp.einsum("jbt,jnt->jbn", hidden_sorted, d_down_rows, preferred_element_type=fp)

    early_stages = 2
    early = dp_reduce_scatter(
        [view(g_left_one), view(g_right_two)], replicas, 0, early_stages
    )
    d_up_inner, *early = lax.optimization_barrier((d_up_inner, *early))
    early = early + mid

    grad_tokens = jnp.einsum(
        "jkgt,kbjg->tkb", d_up_inner, right_one, preferred_element_type=fp
    ).astype(bf)
    grad_tokens = grad_tokens.reshape(tok_rows, in_blocks * block_width)
    d_up_flat = d_up_inner.reshape(all_hid * in_blocks * sub_width, tok_rows)
    tok_sorted = chunk_order(tok_parts[:, 0, :], 1, replicas)
    g_right_one = jnp.einsum("tb,nt->bn", tok_sorted, d_up_flat, preferred_element_type=fp)
    late = [view(g_right_one)]
    stages = len(dp_bit_order(replicas))
    for stage in range(stages):
        late = dp_reduce_scatter(late, replicas, stage, stage + 1)
        if early_stages + stage < stages:
            early = dp_reduce_scatter(early, replicas, early_stages + stage, early_stages + stage + 1)
    red_right_one = late[0][:, 0]
    red_left_one, red_right_two, red_left_two = [e[:, 0] for e in early]
    reduced = (red_right_one, red_left_one, red_right_two, red_left_two)
    grad_right_one, grad_left_one, grad_right_two, grad_left_two = [r * grad_scale for r in reduced]
    return (layer_out, grad_tokens, grad_right_one, grad_left_one, grad_right_two, grad_left_two)


def solution(mesh):
    in_specs = (
        P("dp", "tensor"),
        P("tensor", None, None),
        P("tensor", None, None),
        P("tensor", None, None),
        P("tensor", None, None),
        P("dp", "tensor"),
    )
    out_specs = (
        P("dp", "tensor"),
        P("dp", "tensor"),
        P("tensor", "dp", None),
        P("tensor", "dp", None),
        P("tensor", "dp", None),
        P("tensor", "dp", None),
    )
    return jax.shard_map(layer, mesh=mesh, in_specs=in_specs, out_specs=out_specs, check_vma=False)
```
